256 devices in a mesh: dp: 2 (over core), ctx: 8 (over y, z_lo), feat: 16 (over x, z_hi).
Axes of the slice: x: 4, y: 4, z: 8 (z_hi: 4, z_lo: 2; z = z_hi * 2 + z_lo), core: 2. Of those that a mesh axis runs over, the one named last changes fastest.
Arguments:
- out_grads: bfloat16 [2048, 28672], P(('dp', 'ctx'), 'feat'), may hold values from -6 to 6
- acts: bfloat16 [2048, 8192], P(('dp', 'ctx'), 'feat'), may hold values from -6 to 6
- domain_ids: int32 [2048], P(('dp', 'ctx')), may hold values from 0 to 7
- domain_weights: int32 [8], replicated, may hold values from 1 to 4
Outputs:
- grad_factor: bfloat16 [28672, 28672], P(('dp', 'ctx'), 'feat')
- act_factor: bfloat16 [8192, 8192], P(('dp', 'ctx'), 'feat')
The draws below stay inside these ranges and needn't reach their ends.
All inputs are finite; a program needn't handle non-finite values.
Results may differ from the reference program's by a relative error of at most 0.003.
Values may be sent and summed in bfloat16 or wider, within the bound.
No kernel may reach another device: no remote copies, remote signals or barrier semaphores. Data moves between devices by JAX's collectives and lax.ppermute only.
A program may use at most 128 MiB of HBM per device.

```python
import jax
import jax.numpy as jnp
from jax import lax

D = 8192
FF = 28672
DOMAINS = 8
TOKENS = 2048


def set_ends(array, rng, low, top_value):
    longest = array.shape.index(max(array.shape))
    spots = []
    for shift in (0, 1):
        where = [jax.random.randint(jax.random.fold_in(rng, axis), (), 0, length) for axis, length in enumerate(array.shape)]
        where[longest] = (where[longest] + shift) % array.shape[longest]
        spots.append(tuple(where))
    return array.at[spots[0]].set(low).at[spots[1]].set(top_value)


def spiked(result, own_key, source, target, parts, factor):
    def block_of(position):
        return (jnp.arange(result.shape[position]) // (result.shape[position] // parts)).reshape((-1,) + (1,) * (result.ndim - 1 - position))

    near = jax.random.permutation(own_key, parts)[block_of(target)]
    second = (block_of(target) + parts // 2) % parts
    return jnp.where((block_of(source) == near) | (block_of(source) == second), factor * result, result)


def block_levels(own_key, dims, pieces, smallest, largest):
    factor_of = 1.0
    for dim, shards_of in pieces:
        draws = jax.random.uniform(jax.random.fold_in(jax.random.fold_in(own_key, 6), dim), (shards_of,), jnp.float32, smallest / len(pieces), largest / len(pieces))
        factor_of = factor_of * jnp.repeat(jnp.exp(draws), dims[dim] // shards_of).reshape((-1,) + (1,) * (len(dims) - 1 - dim))
    return factor_of


def scatter_about(own_key, extent, scale, reach, cuts=(), kind=jnp.bfloat16):
    level = block_levels(own_key, extent, cuts, -0.22, 0.18) if cuts else 1.0
    entries = jax.random.normal(own_key, extent, jnp.float32) * scale * level
    return jnp.minimum(jnp.maximum(entries, -reach), reach).astype(kind)


def bell_draw_with(rng, dims, spread, limit, split, heavy, held_as=jnp.bfloat16):
    drawn = spread * jax.random.normal(rng, dims, jnp.float32)
    if split:
        drawn = drawn * block_levels(rng, dims, split, -0.22, 0.18)
    return jnp.clip(spiked(drawn, jax.random.fold_in(rng, 3), *heavy), -limit, limit).astype(held_as)


def setup_inputs(seed: int = 0) -> dict:
    streams_of = jax.random.split(jax.random.key(seed), 5)
    out_grads = bell_draw_with(streams_of[0], (TOKENS, FF), 1.0, 6.0, ((0, 16), (1, 16)), (0, 1, 16, 2.0))
    acts = scatter_about(streams_of[1], (TOKENS, D), 1.0, 6.0, ((0, 16), (1, 16)))
    domain_ids = set_ends(jax.random.randint(streams_of[2], (TOKENS,), 0, DOMAINS), jax.random.fold_in(streams_of[2], 1), 0, DOMAINS - 1).astype(jnp.int32)
    domain_weights = set_ends(jax.random.randint(streams_of[3], (DOMAINS,), 1, 5), jax.random.fold_in(streams_of[3], 1), 1, 4).astype(jnp.int32)
    return {"out_grads": out_grads, "acts": acts, "domain_ids": domain_ids, "domain_weights": domain_weights}


def gram_blocks(rows, weighted, inv_count):
    width = rows.shape[1]
    block_width = 512 if width % 512 == 0 else width
    blocks = width // block_width
    stacked = rows.reshape(rows.shape[0], blocks, block_width).transpose(1, 0, 2)

    def one_block(piece):
        product = jnp.dot(piece.T, weighted, preferred_element_type=jnp.float32)
        return (product * inv_count).astype(jnp.bfloat16)

    return lax.map(one_block, stacked).reshape(width, width)


def reference(out_grads, acts, domain_ids, domain_weights):
    token_weight = domain_weights[domain_ids].astype(jnp.float32)
    weighted_grads = (token_weight[:, None] * out_grads.astype(jnp.float32)).astype(jnp.bfloat16)
    weighted_acts = (token_weight[:, None] * acts.astype(jnp.float32)).astype(jnp.bfloat16)
    inv_count = 1.0 / TOKENS
    grad_factor = gram_blocks(out_grads, weighted_grads, inv_count)
    act_factor = gram_blocks(acts, weighted_acts, inv_count)
    return grad_factor, act_factor
```

```python
import jax
import jax.numpy as jnp
from jax import lax
from jax.sharding import PartitionSpec as P

ROWS = ("dp", "ctx")


def token_weights(tok_ids, domain_weights):
    labels = jnp.arange(domain_weights.shape[0], dtype=jnp.int32)
    match = tok_ids[:, None] == labels[None, :]
    return jnp.sum(jnp.where(match, domain_weights[None, :], 0), axis=1).astype(jnp.float32)


def contract_tokens(left, right):
    return lax.dot_general(
        left, right, (((0,), (0,)), ((), ())), preferred_element_type=jnp.float32
    )


def transpose_pairs(n_rows, n_cols):
    return [(c * n_cols + r, r * n_cols + c) for r in range(n_rows) for c in range(n_cols)]


def local(out_grads, acts, domain_ids, domain_weights):
    n_rows = lax.axis_size(ROWS)
    n_cols = lax.axis_size("feat")
    assert n_rows == n_cols
    inv_count = 1.0 / (out_grads.shape[0] * n_rows)
    width_g = out_grads.shape[1]
    both = jnp.concatenate([out_grads, acts], axis=1)
    tok_weight = token_weights(domain_ids, domain_weights)
    weighted = (tok_weight[:, None] * both.astype(jnp.float32)).astype(jnp.bfloat16)
    cols = lax.all_gather(weighted, ROWS, axis=0, tiled=True)
    swapped = lax.ppermute(both, ROWS + ("feat",), transpose_pairs(n_rows, n_cols))
    rows = lax.all_gather(swapped, "feat", axis=0, tiled=True)
    grad_sum = contract_tokens(rows[:, :width_g], cols[:, :width_g])
    act_sum = contract_tokens(rows[:, width_g:], cols[:, width_g:])
    grad_factor = (grad_sum * inv_count).astype(jnp.bfloat16)
    act_factor = (act_sum * inv_count).astype(jnp.bfloat16)
    return (grad_factor, act_factor)


def solution(mesh):
    in_specs = (P(ROWS, "feat"), P(ROWS, "feat"), P(ROWS), P())
    out_specs = (P(ROWS, "feat"), P(ROWS, "feat"))
    return jax.shard_map(local, mesh=mesh, in_specs=in_specs, out_specs=out_specs, check_vma=False)
```

```python
import jax
import jax.numpy as jnp
from jax import lax
from jax.sharding import PartitionSpec as P

ROWS = ("dp", "ctx")
PAIR = 2


def token_weights(tok_ids, domain_weights):
    labels = jnp.arange(domain_weights.shape[0], dtype=jnp.int32)
    match = tok_ids[:, None] == labels[None, :]
    return jnp.sum(jnp.where(match, domain_weights[None, :], 0), axis=1).astype(jnp.float32)


def contract_tokens(left, right):
    return lax.dot_general(
        left, right, (((0,), (0,)), ((), ())), preferred_element_type=jnp.float32
    )


def split_row(r, n_ring):
    per_dp = n_ring * PAIR
    return r // per_dp, (r % per_dp) // PAIR, r % PAIR


def token_block(r, p, n_dp, n_ring):
    dp, y, z = split_row(r, n_ring)
    ddp, dy, dz = split_row(p, n_ring)
    return ((dp + ddp) % n_dp) * n_ring * PAIR + ((y + dy) % n_ring) * PAIR + (z + dz) % PAIR


def transpose_pairs(n_rows, n_cols, n_dp, n_ring):
    return [(token_block(r, c, n_dp, n_ring) * n_cols + r, r * n_cols + c)
            for r in range(n_rows) for c in range(n_cols)]


def ctx_shift(n_ring, dy, dz):
    pairs = []
    for y in range(n_ring):
        for z in range(PAIR):
            src = ((y + dy) % n_ring) * PAIR + (z + dz) % PAIR
            pairs.append((src, y * PAIR + z))
    return pairs


def gather_columns(block, n_dp, n_ring):
    half = block.shape[0]
    near = lax.ppermute(block, "ctx", ctx_shift(n_ring, 0, 1))
    own = jnp.concatenate([block, near], axis=0)
    ahead = lax.ppermute(own, "ctx", ctx_shift(n_ring, 1, 0))
    behind = lax.ppermute(own, "ctx", ctx_shift(n_ring, -1, 0))
    far_a = lax.ppermute(ahead[:half], "ctx", ctx_shift(n_ring, 1, 0))
    far_b = lax.ppermute(behind[half:], "ctx", ctx_shift(n_ring, -1, 0))
    mine = jnp.concatenate([own, ahead, far_a, far_b, behind], axis=0)
    other = lax.ppermute(mine, "dp", [(1, 0), (0, 1)])
    return jnp.concatenate([mine, other], axis=0)


def local(out_grads, acts, domain_ids, domain_weights):
    n_dp = lax.axis_size("dp")
    n_ctx = lax.axis_size("ctx")
    n_rows = n_dp * n_ctx
    n_cols = lax.axis_size("feat")
    n_ring = n_ctx // PAIR
    assert n_rows == n_cols and n_dp == 2 and n_ring == 4 and n_ctx % PAIR == 0
    inv_count = 1.0 / (out_grads.shape[0] * n_rows)
    width_g = out_grads.shape[1]
    both = jnp.concatenate([out_grads, acts], axis=1)
    tok_weight = token_weights(domain_ids, domain_weights)
    weighted = (tok_weight[:, None] * both.astype(jnp.float32)).astype(jnp.bfloat16)
    swapped = lax.ppermute(both, ROWS + ("feat",), transpose_pairs(n_rows, n_cols, n_dp, n_ring))
    rows = lax.all_gather(swapped, "feat", axis=0, tiled=True)
    cols = gather_columns(weighted, n_dp, n_ring)
    grad_sum = contract_tokens(rows[:, :width_g], cols[:, :width_g])
    act_sum = contract_tokens(rows[:, width_g:], cols[:, width_g:])
    grad_factor = (grad_sum * inv_count).astype(jnp.bfloat16)
    act_factor = (act_sum * inv_count).astype(jnp.bfloat16)
    return (grad_factor, act_factor)


def solution(mesh):
    in_specs = (P(ROWS, "feat"), P(ROWS, "feat"), P(ROWS), P())
    out_specs = (P(ROWS, "feat"), P(ROWS, "feat"))
    return jax.shard_map(local, mesh=mesh, in_specs=in_specs, out_specs=out_specs, check_vma=False)
```

```python
import jax
import jax.numpy as jnp
from jax import lax
from jax.sharding import PartitionSpec as P

ROWS = ("dp", "ctx")
SIDE = 4


def token_weights(tok_ids, domain_weights):
    labels = jnp.arange(domain_weights.shape[0], dtype=jnp.int32)
    match = tok_ids[:, None] == labels[None, :]
    return jnp.sum(jnp.where(match, domain_weights[None, :], 0), axis=1).astype(jnp.float32)


def contract_tokens(left, right):
    return lax.dot_general(
        left, right, (((0,), (0,)), ((), ())), preferred_element_type=jnp.float32
    )


def transpose_pairs(n_rows, n_cols):
    return [(c * n_cols + r, r * n_cols + c) for r in range(n_rows) for c in range(n_cols)]


def feat_shift(dx, dz):
    pairs = []
    for x in range(SIDE):
        for z in range(SIDE):
            pairs.append((((x + dx) % SIDE) * SIDE + (z + dz) % SIDE, x * SIDE + z))
    return pairs


def ring_gather(block, dx, dz):
    half = block.shape[0] // 2
    ahead = lax.ppermute(block, "feat", feat_shift(dx, dz))
    behind = lax.ppermute(block, "feat", feat_shift(-dx, -dz))
    far_a = lax.ppermute(ahead[:half], "feat", feat_shift(dx, dz))
    far_b = lax.ppermute(behind[half:], "feat", feat_shift(-dx, -dz))
    return [block, ahead, jnp.concatenate([far_a, far_b], axis=0), behind]


def gather_rows(piece):
    size = piece.shape[0]
    f = lax.axis_index("feat")
    x, z = f // SIDE, f % SIDE
    line = jnp.concatenate(ring_gather(piece, 0, 1), axis=0)
    rows = jnp.zeros((SIDE * SIDE * size, piece.shape[1]), piece.dtype)
    for dx, block in enumerate(ring_gather(line, 1, 0)):
        for dz in range(SIDE):
            at = (((x + dx) % SIDE) * SIDE + (z + dz) % SIDE) * size
            rows = lax.dynamic_update_slice(rows, block[dz * size:(dz + 1) * size], (at, 0))
    return rows


def local(out_grads, acts, domain_ids, domain_weights):
    n_rows = lax.axis_size(ROWS)
    n_cols = lax.axis_size("feat")
    assert n_rows == n_cols and n_cols == SIDE * SIDE
    inv_count = 1.0 / (out_grads.shape[0] * n_rows)
    width_g = out_grads.shape[1]
    both = jnp.concatenate([out_grads, acts], axis=1)
    tok_weight = token_weights(domain_ids, domain_weights)
    weighted = (tok_weight[:, None] * both.astype(jnp.float32)).astype(jnp.bfloat16)
    cols = lax.all_gather(weighted, ROWS, axis=0, tiled=True)
    swapped = lax.ppermute(both, ROWS + ("feat",), transpose_pairs(n_rows, n_cols))
    rows = gather_rows(swapped)
    grad_sum = contract_tokens(rows[:, :width_g], cols[:, :width_g])
    act_sum = contract_tokens(rows[:, width_g:], cols[:, width_g:])
    grad_factor = (grad_sum * inv_count).astype(jnp.bfloat16)
    act_factor = (act_sum * inv_count).astype(jnp.bfloat16)
    return (grad_factor, act_factor)


def solution(mesh):
    in_specs = (P(ROWS, "feat"), P(ROWS, "feat"), P(ROWS), P())
    out_specs = (P(ROWS, "feat"), P(ROWS, "feat"))
    return jax.shard_map(local, mesh=mesh, in_specs=in_specs, out_specs=out_specs, check_vma=False)
```

```python
import jax
import jax.numpy as jnp
from jax import lax
from jax.sharding import PartitionSpec as P

ROWS = ("dp", "ctx")
PAIR = 2


def token_weights(tok_ids, domain_weights):
    labels = jnp.arange(domain_weights.shape[0], dtype=jnp.int32)
    match = tok_ids[:, None] == labels[None, :]
    return jnp.sum(jnp.where(match, domain_weights[None, :], 0), axis=1).astype(jnp.float32)


def contract_tokens(left, right):
    return lax.dot_general(
        left, right, (((0,), (0,)), ((), ())), preferred_element_type=jnp.float32
    )


def split_row(r, n_ring):
    per_dp = n_ring * PAIR
    return r // per_dp, (r % per_dp) // PAIR, r % PAIR


def token_block(r, p, n_dp, n_ring):
    dp, y, z = split_row(r, n_ring)
    ddp, dy, dz = split_row(p, n_ring)
    return ((dp + ddp) % n_dp) * n_ring * PAIR + ((y + dy) % n_ring) * PAIR + (z + dz) % PAIR


def transpose_pairs(n_rows, n_cols, n_dp, n_ring):
    return [(token_block(r, c, n_dp, n_ring) * n_cols + r, r * n_cols + c)
            for r in range(n_rows) for c in range(n_cols)]


def ctx_shift(n_ring, dy, dz):
    pairs = []
    for y in range(n_ring):
        for z in range(PAIR):
            src = ((y + dy) % n_ring) * PAIR + (z + dz) % PAIR
            pairs.append((src, y * PAIR + z))
    return pairs


def gather_columns(block, n_dp, n_ring):
    half = block.shape[0]
    near = lax.ppermute(block, "ctx", ctx_shift(n_ring, 0, 1))
    own = jnp.concatenate([block, near], axis=0)
    ahead = lax.ppermute(own, "ctx", ctx_shift(n_ring, 1, 0))
    behind = lax.ppermute(own, "ctx", ctx_shift(n_ring, -1, 0))
    far_a = lax.ppermute(ahead[:half], "ctx", ctx_shift(n_ring, 1, 0))
    far_b = lax.ppermute(behind[half:], "ctx", ctx_shift(n_ring, -1, 0))
    mine = jnp.concatenate([own, ahead, far_a, far_b, behind], axis=0)
    other = lax.ppermute(mine, "dp", [(1, 0), (0, 1)])
    return jnp.concatenate([mine, other], axis=0)


def local(out_grads, acts, domain_ids, domain_weights):
    n_dp = lax.axis_size("dp")
    n_ctx = lax.axis_size("ctx")
    n_rows = n_dp * n_ctx
    n_cols = lax.axis_size("feat")
    n_ring = n_ctx // PAIR
    assert n_rows == n_cols and n_dp == 2 and n_ring == 4 and n_ctx % PAIR == 0
    inv_count = 1.0 / (out_grads.shape[0] * n_rows)
    width_g = out_grads.shape[1]
    both = jnp.concatenate([out_grads, acts], axis=1)
    tok_weight = token_weights(domain_ids, domain_weights)
    weighted = (tok_weight[:, None] * both.astype(jnp.float32)).astype(jnp.bfloat16)
    swapped = lax.ppermute(both, ROWS + ("feat",), transpose_pairs(n_rows, n_cols, n_dp, n_ring))
    rows_g = lax.all_gather(swapped[:, :width_g], "feat", axis=0, tiled=True)
    rows_g, piece_a = lax.optimization_barrier((rows_g, swapped[:, width_g:]))
    rows_a = lax.all_gather(piece_a, "feat", axis=0, tiled=True)
    cols = gather_columns(weighted, n_dp, n_ring)
    grad_sum = contract_tokens(rows_g, cols[:, :width_g])
    act_sum = contract_tokens(rows_a, cols[:, width_g:])
    grad_factor = (grad_sum * inv_count).astype(jnp.bfloat16)
    act_factor = (act_sum * inv_count).astype(jnp.bfloat16)
    return (grad_factor, act_factor)


def solution(mesh):
    in_specs = (P(ROWS, "feat"), P(ROWS, "feat"), P(ROWS), P())
    out_specs = (P(ROWS, "feat"), P(ROWS, "feat"))
    return jax.shard_map(local, mesh=mesh, in_specs=in_specs, out_specs=out_specs, check_vma=False)
```

```python
import jax
import jax.numpy as jnp
from jax import lax
from jax.sharding import Mesh
from jax.sharding import PartitionSpec as P

AXES = ("dp", "y", "zlo", "x", "zhi")
ROWS = ("dp", "y", "zlo")
COLS = ("x", "zhi")


def token_weights(tok_ids, domain_weights):
    labels = jnp.arange(domain_weights.shape[0], dtype=jnp.int32)
    match = tok_ids[:, None] == labels[None, :]
    return jnp.sum(jnp.where(match, domain_weights[None, :], 0), axis=1).astype(jnp.float32)


def contract_tokens(left, right):
    return lax.dot_general(
        left, right, (((0,), (0,)), ((), ())), preferred_element_type=jnp.float32
    )


def row_coords(r, n_ring, n_lo):
    per_dp = n_ring * n_lo
    return r // per_dp, (r % per_dp) // n_lo, r % n_lo


def shifted_block(r, ddp, dy, dz, n_dp, n_ring, n_lo):
    dp, y, z = row_coords(r, n_ring, n_lo)
    return ((dp + ddp) % n_dp) * n_ring * n_lo + ((y + dy) % n_ring) * n_lo + (z + dz) % n_lo


def fetch_pairs(k, n_dp, n_ring, n_lo, n_x, n_zh):
    n_rows, n_cols = n_dp * n_ring * n_lo, n_x * n_zh
    pairs = []
    for r in range(n_rows):
        for x in range(n_x):
            for zh in range(n_zh):
                ddp, dz = divmod((k + zh) % (n_dp * n_lo), n_lo)
                s = shifted_block(r, ddp, x, dz, n_dp, n_ring, n_lo)
                pairs.append((s * n_cols + r, r * n_cols + x * n_zh + zh))
    return pairs


def ring_pairs(n_ring, n_lo, dy, dz):
    pairs = []
    for y in range(n_ring):
        for z in range(n_lo):
            pairs.append((((y + dy) % n_ring) * n_lo + (z + dz) % n_lo, y * n_lo + z))
    return pairs


def gather_columns(block, n_ring, n_lo):
    half = block.shape[0]
    near = lax.ppermute(block, ("y", "zlo"), ring_pairs(n_ring, n_lo, 0, 1))
    own = jnp.concatenate([block, near], axis=0)
    ahead = lax.ppermute(own, ("y", "zlo"), ring_pairs(n_ring, n_lo, 1, 0))
    behind = lax.ppermute(own, ("y", "zlo"), ring_pairs(n_ring, n_lo, -1, 0))
    far_a = lax.ppermute(ahead[:half], ("y", "zlo"), ring_pairs(n_ring, n_lo, 1, 0))
    far_b = lax.ppermute(behind[half:], ("y", "zlo"), ring_pairs(n_ring, n_lo, -1, 0))
    mine = jnp.concatenate([own, ahead, far_a, far_b, behind], axis=0)
    other = lax.ppermute(mine, "dp", [(1, 0), (0, 1)])
    width = 2 * half
    parts = []
    for dy in range(n_ring):
        parts += [mine[dy * width:(dy + 1) * width], other[dy * width:(dy + 1) * width]]
    return jnp.concatenate(parts, axis=0)


def local(out_grads, acts, domain_ids, domain_weights):
    n_dp, n_ring, n_lo = (lax.axis_size(a) for a in ROWS)
    n_x, n_zh = (lax.axis_size(a) for a in COLS)
    assert n_dp == 2 and n_lo == 2 and n_ring == n_x and n_dp * n_lo == n_zh
    n_rows = n_dp * n_ring * n_lo
    inv_count = 1.0 / (out_grads.shape[0] * n_rows)
    width_g = out_grads.shape[1]
    both = jnp.concatenate([out_grads, acts], axis=1)
    tok_weight = token_weights(domain_ids, domain_weights)
    weighted = (tok_weight[:, None] * both.astype(jnp.float32)).astype(jnp.bfloat16)
    got = jnp.stack([lax.ppermute(both, AXES, fetch_pairs(k, n_dp, n_ring, n_lo, n_x, n_zh))
                     for k in range(n_zh)])
    zh = lax.axis_index("zhi")
    order = (jnp.arange(n_zh) - zh) % n_zh
    piece = jnp.take(got, order, axis=0).reshape(n_zh * both.shape[0], both.shape[1])
    rows = lax.all_gather(piece, "x", axis=0, tiled=True)
    cols = gather_columns(weighted, n_ring, n_lo)
    grad_sum = contract_tokens(rows[:, :width_g], cols[:, :width_g])
    act_sum = contract_tokens(rows[:, width_g:], cols[:, width_g:])
    grad_factor = (grad_sum * inv_count).astype(jnp.bfloat16)
    act_factor = (act_sum * inv_count).astype(jnp.bfloat16)
    return (grad_factor, act_factor)


def solution(mesh):
    n_dp, n_ctx, n_feat = mesh.devices.shape
    split = Mesh(mesh.devices.reshape(n_dp, n_ctx // 2, 2, 4, n_feat // 4), AXES)
    in_specs = (P(ROWS, COLS), P(ROWS, COLS), P(ROWS), P())
    out_specs = (P(ROWS, COLS), P(ROWS, COLS))
    return jax.shard_map(local, mesh=split, in_specs=in_specs, out_specs=out_specs, check_vma=False)
```

```python
import jax
import jax.numpy as jnp
from jax import lax
from jax.sharding import PartitionSpec as P

ROWS = ("dp", "ctx")
PAIR = 2


def token_weights(tok_ids, domain_weights):
    labels = jnp.arange(domain_weights.shape[0], dtype=jnp.int32)
    match = tok_ids[:, None] == labels[None, :]
    return jnp.sum(jnp.where(match, domain_weights[None, :], 0), axis=1).astype(jnp.float32)


def contract_tokens(left, right):
    return lax.dot_general(
        left, right, (((0,), (0,)), ((), ())), preferred_element_type=jnp.float32
    )


def split_row(r, n_ring):
    per_dp = n_ring * PAIR
    return r // per_dp, (r % per_dp) // PAIR, r % PAIR


def token_block(r, p, n_dp, n_ring):
    dp, y, z = split_row(r, n_ring)
    ddp, dy, dz = split_row(p, n_ring)
    return ((dp + ddp) % n_dp) * n_ring * PAIR + ((y + dy) % n_ring) * PAIR + (z + dz) % PAIR


def transpose_pairs(n_rows, n_cols, n_dp, n_ring):
    return [(token_block(r, c, n_dp, n_ring) * n_cols + r, r * n_cols + c)
            for r in range(n_rows) for c in range(n_cols)]


def ctx_shift(n_ring, dy, dz):
    pairs = []
    for y in range(n_ring):
        for z in range(PAIR):
            src = ((y + dy) % n_ring) * PAIR + (z + dz) % PAIR
            pairs.append((src, y * PAIR + z))
    return pairs


def gather_columns(block, n_dp, n_ring):
    half = block.shape[0]
    near = lax.ppermute(block, "ctx", ctx_shift(n_ring, 0, 1))
    own = jnp.concatenate([block, near], axis=0)
    ahead = lax.ppermute(own, "ctx", ctx_shift(n_ring, 1, 0))
    behind = lax.ppermute(own, "ctx", ctx_shift(n_ring, -1, 0))
    far_a = lax.ppermute(ahead[:half], "ctx", ctx_shift(n_ring, 1, 0))
    far_b = lax.ppermute(behind[half:], "ctx", ctx_shift(n_ring, -1, 0))
    mine = jnp.concatenate([own, ahead, far_a, far_b, behind], axis=0)
    other = lax.ppermute(mine, "dp", [(1, 0), (0, 1)])
    return jnp.concatenate([mine, other], axis=0)


def fetch_pairs(k, n_rows, n_cols, n_dp, n_ring):
    return [(token_block(r, (k + c) % n_cols, n_dp, n_ring) * n_cols + r, r * n_cols + c)
            for r in range(n_rows) for c in range(n_cols)]


def local(out_grads, acts, domain_ids, domain_weights):
    n_dp = lax.axis_size("dp")
    n_ctx = lax.axis_size("ctx")
    n_rows = n_dp * n_ctx
    n_cols = lax.axis_size("feat")
    n_ring = n_ctx // PAIR
    assert n_rows == n_cols and n_dp == 2 and n_ring == 4 and n_ctx % PAIR == 0
    inv_count = 1.0 / (out_grads.shape[0] * n_rows)
    width_g = out_grads.shape[1]
    both = jnp.concatenate([out_grads, acts], axis=1)
    tok_weight = token_weights(domain_ids, domain_weights)
    weighted = (tok_weight[:, None] * both.astype(jnp.float32)).astype(jnp.bfloat16)
    swapped = lax.ppermute(out_grads, ROWS + ("feat",), transpose_pairs(n_rows, n_cols, n_dp, n_ring))
    rows_g = lax.all_gather(swapped, "feat", axis=0, tiled=True)
    got = jnp.stack([lax.ppermute(acts, ROWS + ("feat",), fetch_pairs(k, n_rows, n_cols, n_dp, n_ring))
                     for k in range(n_cols)])
    order = (jnp.arange(n_cols) - lax.axis_index("feat")) % n_cols
    rows_a = jnp.take(got, order, axis=0).reshape(n_cols * acts.shape[0], acts.shape[1])
    cols = gather_columns(weighted, n_dp, n_ring)
    grad_sum = contract_tokens(rows_g, cols[:, :width_g])
    act_sum = contract_tokens(rows_a, cols[:, width_g:])
    grad_factor = (grad_sum * inv_count).astype(jnp.bfloat16)
    act_factor = (act_sum * inv_count).astype(jnp.bfloat16)
    return (grad_factor, act_factor)


def solution(mesh):
    in_specs = (P(ROWS, "feat"), P(ROWS, "feat"), P(ROWS), P())
    out_specs = (P(ROWS, "feat"), P(ROWS, "feat"))
    return jax.shard_map(local, mesh=mesh, in_specs=in_specs, out_specs=out_specs, check_vma=False)
```

```python
import jax
import jax.numpy as jnp
from jax import lax
from jax.sharding import PartitionSpec as P

ROWS = ("dp", "ctx")
PAIR = 2


def token_weights(tok_ids, domain_weights):
    labels = jnp.arange(domain_weights.shape[0], dtype=jnp.int32)
    match = tok_ids[:, None] == labels[None, :]
    return jnp.sum(jnp.where(match, domain_weights[None, :], 0), axis=1).astype(jnp.float32)


def contract_tokens(left, right):
    return lax.dot_general(
        left, right, (((0,), (0,)), ((), ())), preferred_element_type=jnp.float32
    )


def split_row(r, n_ring):
    per_dp = n_ring * PAIR
    return r // per_dp, (r % per_dp) // PAIR, r % PAIR


def token_block(r, p, n_dp, n_ring):
    dp, y, z = split_row(r, n_ring)
    ddp, dy, dz = split_row(p, n_ring)
    return ((dp + ddp) % n_dp) * n_ring * PAIR + ((y + dy) % n_ring) * PAIR + (z + dz) % PAIR


def transpose_pairs(n_rows, n_cols, n_dp, n_ring):
    return [(token_block(r, c, n_dp, n_ring) * n_cols + r, r * n_cols + c)
            for r in range(n_rows) for c in range(n_cols)]


def ctx_shift(n_ring, dy, dz):
    pairs = []
    for y in range(n_ring):
        for z in range(PAIR):
            src = ((y + dy) % n_ring) * PAIR + (z + dz) % PAIR
            pairs.append((src, y * PAIR + z))
    return pairs


def gather_columns(block, n_dp, n_ring):
    half = block.shape[0]
    near = lax.ppermute(block, "ctx", ctx_shift(n_ring, 0, 1))
    own = jnp.concatenate([block, near], axis=0)
    ahead = lax.ppermute(own, "ctx", ctx_shift(n_ring, 1, 0))
    behind = lax.ppermute(own, "ctx", ctx_shift(n_ring, -1, 0))
    far_a = lax.ppermute(ahead[:half], "ctx", ctx_shift(n_ring, 1, 0))
    far_b = lax.ppermute(behind[half:], "ctx", ctx_shift(n_ring, -1, 0))
    mine = jnp.concatenate([own, ahead, far_a, far_b, behind], axis=0)
    other = lax.ppermute(mine, "dp", [(1, 0), (0, 1)])
    return jnp.concatenate([mine, other], axis=0)


def local(out_grads, acts, domain_ids, domain_weights):
    n_dp = lax.axis_size("dp")
    n_ctx = lax.axis_size("ctx")
    n_rows = n_dp * n_ctx
    n_cols = lax.axis_size("feat")
    n_ring = n_ctx // PAIR
    assert n_rows == n_cols and n_dp == 2 and n_ring == 4 and n_ctx % PAIR == 0
    inv_count = 1.0 / (out_grads.shape[0] * n_rows)
    width_g = out_grads.shape[1]
    both = jnp.concatenate([out_grads, acts], axis=1)
    tok_weight = token_weights(domain_ids, domain_weights)
    weighted = (tok_weight[:, None] * both.astype(jnp.float32)).astype(jnp.bfloat16)
    pairs = transpose_pairs(n_rows, n_cols, n_dp, n_ring)
    step = both.shape[0] // 4
    swapped = jnp.concatenate([lax.ppermute(both[i * step:(i + 1) * step], ROWS + ("feat",), pairs)
                               for i in range(4)], axis=0)
    rows = lax.all_gather(swapped, "feat", axis=0, tiled=True)
    cols = gather_columns(weighted, n_dp, n_ring)
    grad_sum = contract_tokens(rows[:, :width_g], cols[:, :width_g])
    act_sum = contract_tokens(rows[:, width_g:], cols[:, width_g:])
    grad_factor = (grad_sum * inv_count).astype(jnp.bfloat16)
    act_factor = (act_sum * inv_count).astype(jnp.bfloat16)
    return (grad_factor, act_factor)


def solution(mesh):
    in_specs = (P(ROWS, "feat"), P(ROWS, "feat"), P(ROWS), P())
    out_specs = (P(ROWS, "feat"), P(ROWS, "feat"))
    return jax.shard_map(local, mesh=mesh, in_specs=in_specs, out_specs=out_specs, check_vma=False)
```

```python
import jax
import jax.numpy as jnp
from jax import lax
from jax.sharding import PartitionSpec as P

ROWS = ("dp", "ctx")
PAIR = 2


def token_weights(tok_ids, domain_weights):
    labels = jnp.arange(domain_weights.shape[0], dtype=jnp.int32)
    match = tok_ids[:, None] == labels[None, :]
    return jnp.sum(jnp.where(match, domain_weights[None, :], 0), axis=1).astype(jnp.float32)


def contract_tokens(left, right):
    return lax.dot_general(
        left, right, (((0,), (0,)), ((), ())), preferred_element_type=jnp.float32
    )


def split_row(r, n_ring):
    per_dp = n_ring * PAIR
    return r // per_dp, (r % per_dp) // PAIR, r % PAIR


def token_block(r, p, n_dp, n_ring):
    dp, y, z = split_row(r, n_ring)
    ddp, dy, dz = split_row(p, n_ring)
    return ((dp + ddp) % n_dp) * n_ring * PAIR + ((y + dy) % n_ring) * PAIR + (z + dz) % PAIR


def transpose_pairs(n_rows, n_cols, n_dp, n_ring):
    return [(token_block(r, c, n_dp, n_ring) * n_cols + r, r * n_cols + c)
            for r in range(n_rows) for c in range(n_cols)]


def ctx_shift(n_ring, dy, dz):
    pairs = []
    for y in range(n_ring):
        for z in range(PAIR):
            src = ((y + dy) % n_ring) * PAIR + (z + dz) % PAIR
            pairs.append((src, y * PAIR + z))
    return pairs


def gather_columns(block, n_dp, n_ring):
    half = block.shape[0]
    near = lax.ppermute(block, "ctx", ctx_shift(n_ring, 0, 1))
    own = jnp.concatenate([block, near], axis=0)
    ahead = lax.ppermute(own, "ctx", ctx_shift(n_ring, 1, 0))
    behind = lax.ppermute(own, "ctx", ctx_shift(n_ring, -1, 0))
    far_a = lax.ppermute(ahead[:half], "ctx", ctx_shift(n_ring, 1, 0))
    far_b = lax.ppermute(behind[half:], "ctx", ctx_shift(n_ring, -1, 0))
    mine = jnp.concatenate([own, ahead, far_a, far_b, behind], axis=0)
    other = lax.ppermute(mine, "dp", [(1, 0), (0, 1)])
    return jnp.concatenate([mine, other], axis=0)


def local(out_grads, acts, domain_ids, domain_weights):
    n_dp = lax.axis_size("dp")
    n_ctx = lax.axis_size("ctx")
    n_rows = n_dp * n_ctx
    n_cols = lax.axis_size("feat")
    n_ring = n_ctx // PAIR
    assert n_rows == n_cols and n_dp == 2 and n_ring == 4 and n_ctx % PAIR == 0
    inv_count = 1.0 / (out_grads.shape[0] * n_rows)
    width_g = out_grads.shape[1]
    both = jnp.concatenate([out_grads, acts], axis=1)
    tok_weight = token_weights(domain_ids, domain_weights)
    weighted = (tok_weight[:, None] * both.astype(jnp.float32)).astype(jnp.bfloat16)
    pairs = transpose_pairs(n_rows, n_cols, n_dp, n_ring)
    swapped = jnp.concatenate([lax.ppermute(out_grads, ROWS + ("feat",), pairs),
                               lax.ppermute(acts, ROWS + ("feat",), pairs)], axis=1)
    rows = lax.all_gather(swapped, "feat", axis=0, tiled=True)
    cols = gather_columns(weighted, n_dp, n_ring)
    grad_sum = contract_tokens(rows[:, :width_g], cols[:, :width_g])
    act_sum = contract_tokens(rows[:, width_g:], cols[:, width_g:])
    grad_factor = (grad_sum * inv_count).astype(jnp.bfloat16)
    act_factor = (act_sum * inv_count).astype(jnp.bfloat16)
    return (grad_factor, act_factor)


def solution(mesh):
    in_specs = (P(ROWS, "feat"), P(ROWS, "feat"), P(ROWS), P())
    out_specs = (P(ROWS, "feat"), P(ROWS, "feat"))
    return jax.shard_map(local, mesh=mesh, in_specs=in_specs, out_specs=out_specs, check_vma=False)
```

```python
import jax
import jax.numpy as jnp
from jax import lax
from jax.sharding import Mesh
from jax.sharding import PartitionSpec as P

AXES = ("dp", "y", "zlo", "x", "zhi")
ROWS = ("dp", "y", "zlo")
COLS = ("x", "zhi")
CTX = ("y", "zlo")
PAIR = 2
SIDE = 4


def token_weights(tok_ids, domain_weights):
    labels = jnp.arange(domain_weights.shape[0], dtype=jnp.int32)
    match = tok_ids[:, None] == labels[None, :]
    return jnp.sum(jnp.where(match, domain_weights[None, :], 0), axis=1).astype(jnp.float32)


def contract_tokens(left, right):
    return lax.dot_general(
        left, right, (((0,), (0,)), ((), ())), preferred_element_type=jnp.float32
    )


def split_row(r, n_ring):
    per_dp = n_ring * PAIR
    return r // per_dp, (r % per_dp) // PAIR, r % PAIR


def token_block(r, p, n_dp, n_ring):
    dp, y, z = split_row(r, n_ring)
    ddp, dy, dz = split_row(p, n_ring)
    return ((dp + ddp) % n_dp) * n_ring * PAIR + ((y + dy) % n_ring) * PAIR + (z + dz) % PAIR


def transpose_pairs(n_rows, n_cols, n_dp, n_ring):
    def place(c):
        return (c % SIDE) * SIDE + c // SIDE
    return [(token_block(r, place(c), n_dp, n_ring) * n_cols + r, r * n_cols + c)
            for r in range(n_rows) for c in range(n_cols)]


def ctx_shift(n_ring, dy, dz):
    pairs = []
    for y in range(n_ring):
        for z in range(PAIR):
            src = ((y + dy) % n_ring) * PAIR + (z + dz) % PAIR
            pairs.append((src, y * PAIR + z))
    return pairs


def gather_columns(block, n_dp, n_ring):
    half = block.shape[0]
    near = lax.ppermute(block, CTX, ctx_shift(n_ring, 0, 1))
    own = jnp.concatenate([block, near], axis=0)
    ahead = lax.ppermute(own, CTX, ctx_shift(n_ring, 1, 0))
    behind = lax.ppermute(own, CTX, ctx_shift(n_ring, -1, 0))
    far_a = lax.ppermute(ahead[:half], CTX, ctx_shift(n_ring, 1, 0))
    far_b = lax.ppermute(behind[half:], CTX, ctx_shift(n_ring, -1, 0))
    mine = jnp.concatenate([own, ahead, far_a, far_b, behind], axis=0)
    other = lax.ppermute(mine, "dp", [(1, 0), (0, 1)])
    return jnp.concatenate([mine, other], axis=0)


def local(out_grads, acts, domain_ids, domain_weights):
    n_dp = lax.axis_size("dp")
    n_ctx = lax.axis_size(CTX)
    n_rows = n_dp * n_ctx
    n_cols = lax.axis_size(COLS)
    assert lax.axis_size("x") == SIDE and lax.axis_size("zhi") == SIDE
    n_ring = n_ctx // PAIR
    assert n_rows == n_cols and n_dp == 2 and n_ring == 4 and n_ctx % PAIR == 0
    inv_count = 1.0 / (out_grads.shape[0] * n_rows)
    width_g = out_grads.shape[1]
    both = jnp.concatenate([out_grads, acts], axis=1)
    tok_weight = token_weights(domain_ids, domain_weights)
    weighted = (tok_weight[:, None] * both.astype(jnp.float32)).astype(jnp.bfloat16)
    pairs = transpose_pairs(n_rows, n_cols, n_dp, n_ring)
    swapped = jnp.concatenate([lax.ppermute(out_grads, AXES, pairs),
                               lax.ppermute(acts, AXES, pairs)], axis=1)
    rows = lax.all_gather(swapped, ("zhi", "x"), axis=0, tiled=True)
    cols = gather_columns(weighted, n_dp, n_ring)
    grad_sum = contract_tokens(rows[:, :width_g], cols[:, :width_g])
    act_sum = contract_tokens(rows[:, width_g:], cols[:, width_g:])
    grad_factor = (grad_sum * inv_count).astype(jnp.bfloat16)
    act_factor = (act_sum * inv_count).astype(jnp.bfloat16)
    return (grad_factor, act_factor)


def solution(mesh):
    n_dp, n_ctx, n_feat = mesh.devices.shape
    split = Mesh(mesh.devices.reshape(n_dp, n_ctx // PAIR, PAIR, n_feat // SIDE, SIDE), AXES)
    in_specs = (P(ROWS, COLS), P(ROWS, COLS), P(ROWS), P())
    out_specs = (P(ROWS, COLS), P(ROWS, COLS))
    return jax.shard_map(local, mesh=split, in_specs=in_specs, out_specs=out_specs, check_vma=False)
```

```python
import jax
import jax.numpy as jnp
from jax import lax
from jax.sharding import PartitionSpec as P

ROWS = ("dp", "ctx")
PAIR = 2


def token_weights(tok_ids, domain_weights):
    labels = jnp.arange(domain_weights.shape[0], dtype=jnp.int32)
    match = tok_ids[:, None] == labels[None, :]
    return jnp.sum(jnp.where(match, domain_weights[None, :], 0), axis=1).astype(jnp.float32)


def contract_tokens(left, right):
    return lax.dot_general(
        left, right, (((0,), (0,)), ((), ())), preferred_element_type=jnp.float32
    )


def split_row(r, n_ring):
    per_dp = n_ring * PAIR
    return r // per_dp, (r % per_dp) // PAIR, r % PAIR


def token_block(r, p, n_dp, n_ring):
    dp, y, z = split_row(r, n_ring)
    ddp, dy, dz = split_row(p, n_ring)
    return ((dp + ddp) % n_dp) * n_ring * PAIR + ((y + dy) % n_ring) * PAIR + (z + dz) % PAIR


def transpose_pairs(n_rows, n_cols, n_dp, n_ring):
    return [(token_block(r, c, n_dp, n_ring) * n_cols + r, r * n_cols + c)
            for r in range(n_rows) for c in range(n_cols)]


def ctx_shift(n_ring, dy, dz):
    pairs = []
    for y in range(n_ring):
        for z in range(PAIR):
            src = ((y + dy) % n_ring) * PAIR + (z + dz) % PAIR
            pairs.append((src, y * PAIR + z))
    return pairs


def gather_columns(block, n_dp, n_ring):
    half = block.shape[0]
    near = lax.ppermute(block, "ctx", ctx_shift(n_ring, 0, 1))
    own = jnp.concatenate([block, near], axis=0)
    ahead = lax.ppermute(own, "ctx", ctx_shift(n_ring, 1, 0))
    behind = lax.ppermute(own, "ctx", ctx_shift(n_ring, -1, 0))
    far_a = lax.ppermute(ahead[:half], "ctx", ctx_shift(n_ring, 1, 0))
    far_b = lax.ppermute(behind[half:], "ctx", ctx_shift(n_ring, -1, 0))
    mine = jnp.concatenate([own, ahead, far_a, far_b, behind], axis=0)
    other = lax.ppermute(mine, "dp", [(1, 0), (0, 1)])
    return jnp.concatenate([mine, other], axis=0)


def local(out_grads, acts, domain_ids, domain_weights):
    n_dp = lax.axis_size("dp")
    n_ctx = lax.axis_size("ctx")
    n_rows = n_dp * n_ctx
    n_cols = lax.axis_size("feat")
    n_ring = n_ctx // PAIR
    assert n_rows == n_cols and n_dp == 2 and n_ring == 4 and n_ctx % PAIR == 0
    inv_count = 1.0 / (out_grads.shape[0] * n_rows)
    width_g = out_grads.shape[1]
    both = jnp.concatenate([out_grads, acts], axis=1)
    tok_weight = token_weights(domain_ids, domain_weights)
    weighted = (tok_weight[:, None] * both.astype(jnp.float32)).astype(jnp.bfloat16)
    pairs = transpose_pairs(n_rows, n_cols, n_dp, n_ring)
    swapped = lax.ppermute(out_grads, ROWS + ("feat",), pairs)
    rows_g = lax.all_gather(swapped, "feat", axis=0, tiled=True)
    cols = gather_columns(jnp.concatenate([weighted, acts], axis=1), n_dp, n_ring)
    width = both.shape[1]
    plain = [(c * n_cols + r, r * n_cols + c) for r in range(n_rows) for c in range(n_cols)]
    got = lax.ppermute(cols[:, width:], ROWS + ("feat",), plain)
    r_dp, r_y, r_z = split_row(lax.axis_index(ROWS), n_ring)
    c_dp, c_y, c_z = split_row(lax.axis_index("feat"), n_ring)
    ddp, dy, dz = split_row(jnp.arange(n_rows), n_ring)
    src = (((r_dp - c_dp + ddp) % n_dp) * n_ring * PAIR + ((r_y - c_y + dy) % n_ring) * PAIR
           + (r_z - c_z + dz) % PAIR)
    block = acts.shape[0]
    rows_a = jnp.take(got.reshape(n_rows, block, acts.shape[1]), src, axis=0).reshape(got.shape)
    grad_sum = contract_tokens(rows_g, cols[:, :width_g])
    act_sum = contract_tokens(rows_a, cols[:, width_g:width])
    grad_factor = (grad_sum * inv_count).astype(jnp.bfloat16)
    act_factor = (act_sum * inv_count).astype(jnp.bfloat16)
    return (grad_factor, act_factor)


def solution(mesh):
    in_specs = (P(ROWS, "feat"), P(ROWS, "feat"), P(ROWS), P())
    out_specs = (P(ROWS, "feat"), P(ROWS, "feat"))
    return jax.shard_map(local, mesh=mesh, in_specs=in_specs, out_specs=out_specs, check_vma=False)
```

```python
import jax
import jax.numpy as jnp
from jax import lax
from jax.sharding import PartitionSpec as P

ROWS = ("dp", "ctx")
PAIR = 2


def token_weights(tok_ids, domain_weights):
    labels = jnp.arange(domain_weights.shape[0], dtype=jnp.int32)
    match = tok_ids[:, None] == labels[None, :]
    return jnp.sum(jnp.where(match, domain_weights[None, :], 0), axis=1).astype(jnp.float32)


def contract_tokens(left, right):
    return lax.dot_general(
        left, right, (((0,), (0,)), ((), ())), preferred_element_type=jnp.float32
    )


def split_row(r, n_ring):
    per_dp = n_ring * PAIR
    return r // per_dp, (r % per_dp) // PAIR, r % PAIR


def token_block(r, p, n_dp, n_ring):
    dp, y, z = split_row(r, n_ring)
    ddp, dy, dz = split_row(p, n_ring)
    return ((dp + ddp) % n_dp) * n_ring * PAIR + ((y + dy) % n_ring) * PAIR + (z + dz) % PAIR


def transpose_pairs(n_rows, n_cols, n_dp, n_ring):
    return [(token_block(r, c, n_dp, n_ring) * n_cols + r, r * n_cols + c)
            for r in range(n_rows) for c in range(n_cols)]


def ctx_shift(n_ring, dy, dz):
    pairs = []
    for y in range(n_ring):
        for z in range(PAIR):
            src = ((y + dy) % n_ring) * PAIR + (z + dz) % PAIR
            pairs.append((src, y * PAIR + z))
    return pairs


def gather_columns(block, n_dp, n_ring):
    half = block.shape[0]
    near = lax.ppermute(block, "ctx", ctx_shift(n_ring, 0, 1))
    own = jnp.concatenate([block, near], axis=0)
    ahead = lax.ppermute(own, "ctx", ctx_shift(n_ring, 1, 0))
    behind = lax.ppermute(own, "ctx", ctx_shift(n_ring, -1, 0))
    far_a = lax.ppermute(ahead[:half], "ctx", ctx_shift(n_ring, 1, 0))
    far_b = lax.ppermute(behind[half:], "ctx", ctx_shift(n_ring, -1, 0))
    mine = jnp.concatenate([own, ahead, far_a, far_b, behind], axis=0)
    other = lax.ppermute(mine, "dp", [(1, 0), (0, 1)])
    return jnp.concatenate([mine, other], axis=0)


def local(out_grads, acts, domain_ids, domain_weights):
    n_dp = lax.axis_size("dp")
    n_ctx = lax.axis_size("ctx")
    n_rows = n_dp * n_ctx
    n_cols = lax.axis_size("feat")
    n_ring = n_ctx // PAIR
    assert n_rows == n_cols and n_dp == 2 and n_ring == 4 and n_ctx % PAIR == 0
    inv_count = 1.0 / (out_grads.shape[0] * n_rows)
    width_g = out_grads.shape[1]
    both = jnp.concatenate([out_grads, acts], axis=1)
    tok_weight = token_weights(domain_ids, domain_weights)
    weighted = (tok_weight[:, None] * both.astype(jnp.float32)).astype(jnp.bfloat16)
    pairs = transpose_pairs(n_rows, n_cols, n_dp, n_ring)
    swapped = jnp.concatenate([lax.ppermute(out_grads, ROWS + ("feat",), pairs),
                               lax.ppermute(acts, ROWS + ("feat",), pairs)], axis=1)
    rows = lax.all_gather(swapped, "feat", axis=0, tiled=True)
    cols = gather_columns(weighted, n_dp, n_ring)
    grad_sum = contract_tokens(rows[:, :width_g], cols[:, :width_g])
    act_sum = contract_tokens(rows[:, width_g:], lax.optimization_barrier(cols[:, width_g:]))
    grad_factor = (grad_sum * inv_count).astype(jnp.bfloat16)
    act_factor = (act_sum * inv_count).astype(jnp.bfloat16)
    return (grad_factor, act_factor)


def solution(mesh):
    in_specs = (P(ROWS, "feat"), P(ROWS, "feat"), P(ROWS), P())
    out_specs = (P(ROWS, "feat"), P(ROWS, "feat"))
    return jax.shard_map(local, mesh=mesh, in_specs=in_specs, out_specs=out_specs, check_vma=False)
```
